32 devices in a mesh: groups: 2 (over y), filt: 4 (over z), patch: 4 (over x, core).
Axes of the slice: x: 2, y: 2, z: 4, core: 2. Of those that a mesh axis runs over, the one named last changes fastest.
Arguments:
- activations: bfloat16 [8, 256, 4, 128, 128], P(('groups', 'patch'), None, None, 'filt'), parts along dimension 0, may hold values from -6 to 6
- filters: bfloat16 [3, 3, 3, 256, 256], replicated, may hold values from -0.078125 to 0.078125
- bias: bfloat16 [256], replicated, may hold values from -3 to 3
- cotangent: bfloat16 [8, 256, 4, 128, 128], P(('groups', 'patch'), None, None, 'filt'), parts along dimension 0, may hold values from -6 to 6
Outputs:
- output: bfloat16 [8, 256, 4, 128, 128], P(('groups', 'patch'), None, None, 'filt'), parts along dimension 0
- filter_grad: float32 [6, 3, 3, 256, 256], P('groups', None, None, None, 'filt'), parts along dimension 0
- bias_grad: float32 [512], P(('groups', 'filt')), parts along dimension 0
The draws below stay inside these ranges and needn't reach their ends.
There are 2 independent parts, one for each index of `groups`. The reference program is written for one: setup_inputs(seed, part) draws one part's arguments, and reference() takes and returns one part's arrays. A program takes and returns all parts, laid end to end along the dimension named above; an argument that names none is the same for every part. Nothing has to cross between parts.
All inputs are finite; a program needn't handle non-finite values.
Results may differ from the reference program's by a relative error of at most 0.001.
Values may be sent and summed in bfloat16 or wider, within the bound.
No kernel may reach another device: no remote copies, remote signals or barrier semaphores. Data moves between devices by JAX's collectives and lax.ppermute only.
A program may use at most 640 MiB of HBM per device.

```python
import math
import jax
import jax.numpy as jnp
from jax import lax

CH = 256
DEP = 4
HH = 128
WW = 128
PATCHES = 4


def block_levels(own_key, dims, shards, smallest, high):
    def one(axis_at, blocks):
        heights = jax.random.uniform(jax.random.fold_in(jax.random.fold_in(own_key, 6), axis_at), (blocks,), jnp.float32, smallest / len(shards), high / len(shards))
        return jnp.repeat(jnp.exp(heights), dims[axis_at] // blocks).reshape((-1,) + (1,) * (len(dims) - axis_at - 1))

    loudness = one(*shards[0])
    for cut in shards[1:]:
        loudness = loudness * one(*cut)
    return loudness


def bell_draw(own_key, dims, width, reach, split=(), held_as=jnp.bfloat16):
    values = width * jax.random.normal(own_key, dims, jnp.float32)
    if split:
        values = values * block_levels(own_key, dims, split, -0.22, 0.18)
    return jnp.clip(values, -reach, reach).astype(held_as)


def setup_inputs(seed: int = 0, part: int = 0) -> dict:
    key_list = jax.random.split(jax.random.key(seed), 5)
    part_splits = jax.random.split(jax.random.fold_in(key_list[4], part), 5)
    return {
        "activations": bell_draw(part_splits[0], (PATCHES, CH, DEP, HH, WW), 1.0, 6.0, ((0, 4), (3, 4))),
        "filters": bell_draw(key_list[1], (3, 3, 3, CH, CH), (27 * CH) ** -0.5, 0.078125),
        "bias": bell_draw(key_list[2], (CH,), 0.5, 3.0),
        "cotangent": bell_draw(part_splits[3], (PATCHES, CH, DEP, HH, WW), 1.0, 6.0, ((0, 4), (3, 4))),
    }


def reference(activations, filters, bias, cotangent):
    inputs = activations.astype(jnp.float32)
    grads_in = cotangent.astype(jnp.float32)
    weights = filters.astype(jnp.float32)
    padded = jnp.pad(inputs, ((0, 0), (0, 0), (1, 1), (1, 1), (1, 1)))
    accum = jnp.zeros(grads_in.shape, jnp.float32)
    pieces = []
    for tap_a in range(3):
        for tap_b in range(3):
            for tap_c in range(3):
                window = padded[:, :, tap_a:tap_a + DEP, tap_b:tap_b + HH, tap_c:tap_c + WW]
                accum = accum + jnp.einsum('pidhw,io->podhw', window, weights[tap_a, tap_b, tap_c])
                pieces.append(jnp.einsum('pidhw,podhw->io', window, grads_in))
    output = (accum + bias.astype(jnp.float32)[None, :, None, None, None]).astype(jnp.bfloat16)
    scale = jnp.float32(1.0 / math.sqrt(PATCHES * DEP * HH * WW))
    filter_grad = jnp.stack(pieces).reshape(3, 3, 3, CH, CH) * scale
    bias_grad = lax.optimization_barrier(jnp.sum(grads_in, axis=(0, 2, 3, 4))) * scale
    return (output, filter_grad, bias_grad)
```

```python
import functools
import math

import jax
import jax.numpy as jnp
from jax import lax
from jax.experimental import pallas as pl
from jax.experimental.pallas import tpu as pltpu
from jax.sharding import PartitionSpec as P


def padded_2(cells, sides, width):
    for axis, dim in sides:
        count = lax.axis_size(axis)
        ends = count - 1
        head = lax.slice_in_dim(cells, 0, width, axis=dim)
        tail = lax.slice_in_dim(cells, cells.shape[dim] - width, cells.shape[dim], axis=dim)
        cells = jnp.concatenate(
            [
                lax.ppermute(tail, axis, [(i, (i + 1) % count) for i in range(ends)]),
                cells,
                lax.ppermute(head, axis, [((i + 1) % count, i) for i in range(ends)]),
            ],
            axis=dim,
        )
    return cells


def _wgrad_kernel(depth, lanes, x_ref, g_ref, o_ref):
    e = pl.program_id(0)
    a = pl.program_id(1)
    d = e + 1 - a

    @pl.when((e == 0) & (a == 0))
    def _():
        o_ref[...] = jnp.zeros_like(o_ref)

    @pl.when((d >= 0) & (d < depth))
    def _():
        g = g_ref[0]
        for b in range(3):
            win = x_ref[0, :, pl.ds(128 * b, lanes)]
            o_ref[a, b] += lax.dot_general(
                win, g, (((1,), (1,)), ((), ())), preferred_element_type=jnp.float32
            )


def wgrad(xc, gp):
    depth, rows3, lanes_h = xc.shape
    _, chans, lanes = gp.shape
    cost = pl.CostEstimate(
        flops=2 * 9 * depth * 3 * rows3 * chans * lanes // 3 * 3,
        bytes_accessed=xc.size * 2 + gp.size * 2 * 3 + 9 * rows3 * chans * 4,
        transcendentals=0,
    )
    return pl.pallas_call(
        functools.partial(_wgrad_kernel, depth, lanes),
        grid=(depth, 3),
        in_specs=[
            pl.BlockSpec((1, rows3, lanes_h), lambda e, a: (e, 0, 0)),
            pl.BlockSpec(
                (1, chans, lanes),
                lambda e, a: (jnp.clip(e + 1 - a, 0, depth - 1), 0, 0),
            ),
        ],
        out_specs=pl.BlockSpec((3, 3, rows3, chans), lambda e, a: (0, 0, 0, 0)),
        out_shape=jax.ShapeDtypeStruct((3, 3, rows3, chans), jnp.float32),
        compiler_params=pltpu.CompilerParams(
            dimension_semantics=("arbitrary", "arbitrary"),
            vmem_limit_bytes=60 * 1024 * 1024,
        ),
        cost_estimate=cost,
    )(xc, gp)


def local(activations, filters, bias, cotangent):
    count, channels, depth, rows, width = activations.shape
    n_filt = lax.axis_size("filt")
    n_patch = lax.axis_size("patch")
    owned = channels // n_filt
    piece = owned // n_patch
    scale = 1.0 / math.sqrt(count * n_patch * depth * rows * n_filt * width)
    rimmed = padded_2(activations, (("filt", 3),), 1)
    accum = lax.conv_general_dilated(
        rimmed,
        filters,
        window_strides=(1, 1, 1),
        padding=((1, 1), (0, 0), (1, 1)),
        dimension_numbers=("NCDHW", "DHWIO", "NCDHW"),
        preferred_element_type=jnp.float32,
    )
    output = (accum + bias.astype(jnp.float32)[None, :, None, None, None]).astype(jnp.bfloat16)
    wide = jnp.pad(rimmed[0], ((0, 0), (0, 0), (0, 0), (1, 1)))
    shifts = jnp.stack([wide[..., c : c + width] for c in range(3)])
    xc = jnp.transpose(shifts, (2, 0, 1, 3, 4)).reshape(depth, 3 * channels, (rows + 2) * width)
    gp = cotangent[0].reshape(n_filt, n_patch, piece, depth, rows, width)
    gp = jnp.transpose(gp, (3, 1, 0, 2, 4, 5)).reshape(depth, channels, rows * width)
    grads_all = wgrad(xc, gp)
    grads = jnp.transpose(grads_all.reshape(27 * channels, channels), (1, 0))
    grads = grads.reshape(n_patch * n_filt, piece * 27, channels)
    grads = lax.psum_scatter(grads, ("patch", "filt"), scatter_dimension=0, tiled=True)
    grads = lax.all_gather(grads, "patch", axis=0, tiled=True)
    grads = grads.reshape(owned, 3, 3, 3, channels)
    filter_grad = jnp.transpose(grads, (1, 2, 3, 4, 0)) * scale
    bias_all = jnp.sum(cotangent.astype(jnp.float32), axis=(0, 2, 3, 4))
    bias_part = lax.psum_scatter(bias_all, "filt", scatter_dimension=0, tiled=True)
    bias_part = lax.psum(bias_part, "patch")
    return (output, filter_grad, bias_part * scale)


def solution(mesh):
    return jax.shard_map(
        local,
        mesh=mesh,
        in_specs=(
            P(("groups", "patch"), None, None, "filt", None),
            P(),
            P(),
            P(("groups", "patch"), None, None, "filt", None),
        ),
        out_specs=(
            P(("groups", "patch"), None, None, "filt", None),
            P("groups", None, None, None, "filt"),
            P(("groups", "filt")),
        ),
        check_vma=False,
    )
```

```python
import functools
import math

import jax
import jax.numpy as jnp
from jax import lax
from jax.experimental import pallas as pl
from jax.experimental.pallas import tpu as pltpu
from jax.sharding import PartitionSpec as P


def padded_2(cells, sides, width):
    for axis, dim in sides:
        count = lax.axis_size(axis)
        ends = count - 1
        head = lax.slice_in_dim(cells, 0, width, axis=dim)
        tail = lax.slice_in_dim(cells, cells.shape[dim] - width, cells.shape[dim], axis=dim)
        cells = jnp.concatenate(
            [
                lax.ppermute(tail, axis, [(i, (i + 1) % count) for i in range(ends)]),
                cells,
                lax.ppermute(head, axis, [((i + 1) % count, i) for i in range(ends)]),
            ],
            axis=dim,
        )
    return cells


def _wgrad_kernel(depth, lanes, x_ref, g_ref, o_ref):
    e = pl.program_id(0)
    a = pl.program_id(1)
    d = e + 1 - a

    @pl.when((e == 0) & (a == 0))
    def _():
        o_ref[...] = jnp.zeros_like(o_ref)

    @pl.when((d >= 0) & (d < depth))
    def _():
        g = g_ref[0]
        for b in range(3):
            win = x_ref[0, :, pl.ds(128 * b, lanes)]
            o_ref[a, b] += lax.dot_general(
                win, g, (((1,), (1,)), ((), ())), preferred_element_type=jnp.float32
            )


def wgrad(xc, gp):
    depth, rows3, lanes_h = xc.shape
    _, chans, lanes = gp.shape
    cost = pl.CostEstimate(
        flops=2 * 9 * depth * 3 * rows3 * chans * lanes // 3 * 3,
        bytes_accessed=xc.size * 2 + gp.size * 2 * 3 + 9 * rows3 * chans * 4,
        transcendentals=0,
    )
    return pl.pallas_call(
        functools.partial(_wgrad_kernel, depth, lanes),
        grid=(depth, 3),
        in_specs=[
            pl.BlockSpec((1, rows3, lanes_h), lambda e, a: (e, 0, 0)),
            pl.BlockSpec(
                (1, chans, lanes),
                lambda e, a: (jnp.clip(e + 1 - a, 0, depth - 1), 0, 0),
            ),
        ],
        out_specs=pl.BlockSpec((3, 3, rows3, chans), lambda e, a: (0, 0, 0, 0)),
        out_shape=jax.ShapeDtypeStruct((3, 3, rows3, chans), jnp.float32),
        compiler_params=pltpu.CompilerParams(
            dimension_semantics=("arbitrary", "arbitrary"),
            vmem_limit_bytes=60 * 1024 * 1024,
        ),
        cost_estimate=cost,
    )(xc, gp)


def local(activations, filters, bias, cotangent):
    count, channels, depth, rows, width = activations.shape
    n_filt = lax.axis_size("filt")
    n_patch = lax.axis_size("patch")
    owned = channels // n_filt
    piece = owned // n_patch
    scale = 1.0 / math.sqrt(count * n_patch * depth * rows * n_filt * width)
    rimmed = padded_2(activations, (("filt", 3),), 1)
    accum = lax.conv_general_dilated(
        rimmed,
        filters,
        window_strides=(1, 1, 1),
        padding=((1, 1), (0, 0), (1, 1)),
        dimension_numbers=("NCDHW", "DHWIO", "NCDHW"),
        preferred_element_type=jnp.float32,
    )
    output = (accum + bias.astype(jnp.float32)[None, :, None, None, None]).astype(jnp.bfloat16)
    lanes_h = (rows + 2) * width
    flat = jnp.transpose(rimmed[0], (1, 0, 2, 3)).reshape(depth, channels, lanes_h)
    wide = jnp.pad(flat, ((0, 0), (0, 0), (1, 1)))
    column = lax.broadcasted_iota(jnp.int32, (1, 1, lanes_h), 2) % width
    zero = jnp.zeros((), flat.dtype)
    left = jnp.where(column == 0, zero, wide[..., 0:lanes_h])
    right = jnp.where(column == width - 1, zero, wide[..., 2 : lanes_h + 2])
    xc = jnp.concatenate([left, flat, right], axis=1)
    gp = cotangent[0].reshape(n_filt, n_patch, piece, depth, rows, width)
    gp = jnp.transpose(gp, (3, 1, 0, 2, 4, 5)).reshape(depth, channels, rows * width)
    grads_all = wgrad(xc, gp)
    grads = jnp.transpose(grads_all.reshape(27 * channels, channels), (1, 0))
    grads = grads.reshape(n_patch * n_filt, piece * 27, channels)
    bias_all = jnp.sum(cotangent.astype(jnp.float32), axis=(0, 2, 3, 4))
    bias_all = jnp.transpose(bias_all.reshape(n_filt, n_patch, piece), (1, 0, 2))
    bias_row = jnp.pad(bias_all.reshape(n_patch * n_filt, 1, piece), ((0, 0), (0, 0), (0, channels - piece)))
    grads = jnp.concatenate([grads, bias_row], axis=1)
    grads = lax.psum_scatter(grads, ("patch", "filt"), scatter_dimension=0, tiled=True)
    grads = lax.all_gather(grads, "patch", axis=0, tiled=True)
    bias_part = grads[:, piece * 27, :piece].reshape(owned)
    grads = grads[:, : piece * 27, :].reshape(owned, 3, 3, 3, channels)
    filter_grad = jnp.transpose(grads, (1, 2, 3, 4, 0)) * scale
    return (output, filter_grad, bias_part * scale)


def solution(mesh):
    return jax.shard_map(
        local,
        mesh=mesh,
        in_specs=(
            P(("groups", "patch"), None, None, "filt", None),
            P(),
            P(),
            P(("groups", "patch"), None, None, "filt", None),
        ),
        out_specs=(
            P(("groups", "patch"), None, None, "filt", None),
            P("groups", None, None, None, "filt"),
            P(("groups", "filt")),
        ),
        check_vma=False,
    )
```

```python
import functools
import math

import jax
import jax.numpy as jnp
from jax import lax
from jax.experimental import pallas as pl
from jax.experimental.pallas import tpu as pltpu
from jax.sharding import PartitionSpec as P


def padded_2(cells, sides, width):
    for axis, dim in sides:
        count = lax.axis_size(axis)
        ends = count - 1
        head = lax.slice_in_dim(cells, 0, width, axis=dim)
        tail = lax.slice_in_dim(cells, cells.shape[dim] - width, cells.shape[dim], axis=dim)
        cells = jnp.concatenate(
            [
                lax.ppermute(tail, axis, [(i, (i + 1) % count) for i in range(ends)]),
                cells,
                lax.ppermute(head, axis, [((i + 1) % count, i) for i in range(ends)]),
            ],
            axis=dim,
        )
    return cells


def _wgrad_kernel(depth, lanes, x_ref, g_ref, o_ref, acc_ref, bias_ref):
    e = pl.program_id(0)
    a = pl.program_id(1)
    d = e + 1 - a
    rows3 = x_ref.shape[1]

    @pl.when((e == 0) & (a == 0))
    def _():
        acc_ref[...] = jnp.zeros_like(acc_ref)
        bias_ref[...] = jnp.zeros_like(bias_ref)

    @pl.when((d >= 0) & (d < depth))
    def _():
        g = g_ref[0]
        for b in range(3):
            win = x_ref[0, :, pl.ds(128 * b, lanes)]
            acc_ref[a, b] += lax.dot_general(
                win, g, (((1,), (1,)), ((), ())), preferred_element_type=jnp.float32
            )

    @pl.when(a == 1)
    def _():
        sums = jnp.sum(g_ref[0].astype(jnp.float32), axis=1, keepdims=True)
        bias_ref[...] += jnp.broadcast_to(sums, bias_ref.shape)

    @pl.when((e == depth - 1) & (a == 2))
    def _():
        for ta in range(3):
            for tb in range(3):
                at = (ta * 3 + tb) * rows3
                o_ref[:, at : at + rows3] = acc_ref[ta, tb].T
        o_ref[:, 9 * rows3 :] = bias_ref[...]


def wgrad(xc, gp):
    depth, rows3, lanes_h = xc.shape
    _, chans, lanes = gp.shape
    width_out = 9 * rows3 + 128
    cost = pl.CostEstimate(
        flops=2 * 9 * depth * rows3 * chans * lanes,
        bytes_accessed=xc.size * 2 + gp.size * 2 * 3 + chans * width_out * 4,
        transcendentals=0,
    )
    return pl.pallas_call(
        functools.partial(_wgrad_kernel, depth, lanes),
        grid=(depth, 3),
        in_specs=[
            pl.BlockSpec((1, rows3, lanes_h), lambda e, a: (e, 0, 0)),
            pl.BlockSpec(
                (1, chans, lanes),
                lambda e, a: (jnp.clip(e + 1 - a, 0, depth - 1), 0, 0),
            ),
        ],
        out_specs=pl.BlockSpec((chans, width_out), lambda e, a: (0, 0)),
        out_shape=jax.ShapeDtypeStruct((chans, width_out), jnp.float32),
        scratch_shapes=[
            pltpu.VMEM((3, 3, rows3, chans), jnp.float32),
            pltpu.VMEM((chans, 128), jnp.float32),
        ],
        compiler_params=pltpu.CompilerParams(
            dimension_semantics=("arbitrary", "arbitrary"),
            vmem_limit_bytes=60 * 1024 * 1024,
        ),
        cost_estimate=cost,
    )(xc, gp)


def local(activations, filters, bias, cotangent):
    count, channels, depth, rows, width = activations.shape
    n_filt = lax.axis_size("filt")
    n_patch = lax.axis_size("patch")
    owned = channels // n_filt
    piece = owned // n_patch
    scale = 1.0 / math.sqrt(count * n_patch * depth * rows * n_filt * width)
    rimmed = padded_2(activations, (("filt", 3),), 1)
    accum = lax.conv_general_dilated(
        rimmed,
        filters,
        window_strides=(1, 1, 1),
        padding=((1, 1), (0, 0), (1, 1)),
        dimension_numbers=("NCDHW", "DHWIO", "NCDHW"),
        preferred_element_type=jnp.float32,
    )
    output = (accum + bias.astype(jnp.float32)[None, :, None, None, None]).astype(jnp.bfloat16)
    lanes_h = (rows + 2) * width
    flat = jnp.transpose(rimmed[0], (1, 0, 2, 3)).reshape(depth, channels, lanes_h)
    wide = jnp.pad(flat, ((0, 0), (0, 0), (1, 1)))
    column = lax.broadcasted_iota(jnp.int32, (1, 1, lanes_h), 2) % width
    zero = jnp.zeros((), flat.dtype)
    left = jnp.where(column == 0, zero, wide[..., 0:lanes_h])
    right = jnp.where(column == width - 1, zero, wide[..., 2 : lanes_h + 2])
    xc = jnp.concatenate([left, flat, right], axis=1)
    gp = cotangent[0].reshape(n_filt, n_patch, piece, depth, rows, width)
    gp = jnp.transpose(gp, (3, 1, 0, 2, 4, 5)).reshape(depth, channels, rows * width)
    grads_t = wgrad(xc, gp)
    span = grads_t.shape[1]
    taps = 27 * channels
    grads = grads_t.reshape(n_patch * n_filt, piece, span)
    grads = lax.psum_scatter(grads, ("patch", "filt"), scatter_dimension=0, tiled=True)
    grads = lax.all_gather(grads, "patch", axis=0, tiled=True)
    bias_part = grads[:, :, taps].reshape(owned)
    grads = grads[:, :, :taps].reshape(owned, 27, channels)
    filter_grad = jnp.transpose(grads, (1, 2, 0)).reshape(3, 3, 3, channels, owned) * scale
    return (output, filter_grad, bias_part * scale)


def solution(mesh):
    return jax.shard_map(
        local,
        mesh=mesh,
        in_specs=(
            P(("groups", "patch"), None, None, "filt", None),
            P(),
            P(),
            P(("groups", "patch"), None, None, "filt", None),
        ),
        out_specs=(
            P(("groups", "patch"), None, None, "filt", None),
            P("groups", None, None, None, "filt"),
            P(("groups", "filt")),
        ),
        check_vma=False,
    )
```

```python
import functools
import math

import jax
import jax.numpy as jnp
from jax import lax
from jax.experimental import pallas as pl
from jax.experimental.pallas import tpu as pltpu
from jax.sharding import PartitionSpec as P


def padded_2(cells, sides, width):
    for axis, dim in sides:
        count = lax.axis_size(axis)
        ends = count - 1
        head = lax.slice_in_dim(cells, 0, width, axis=dim)
        tail = lax.slice_in_dim(cells, cells.shape[dim] - width, cells.shape[dim], axis=dim)
        cells = jnp.concatenate(
            [
                lax.ppermute(tail, axis, [(i, (i + 1) % count) for i in range(ends)]),
                cells,
                lax.ppermute(head, axis, [((i + 1) % count, i) for i in range(ends)]),
            ],
            axis=dim,
        )
    return cells


def _wgrad_kernel(depth, lanes, xl_ref, xm_ref, xr_ref, g_ref, o_ref, x_ref, acc_ref, bias_ref):
    e = pl.program_id(0)
    a = pl.program_id(1)
    d = e + 1 - a
    chans = xm_ref.shape[1]
    rows3 = 3 * chans

    @pl.when((e == 0) & (a == 0))
    def _():
        acc_ref[...] = jnp.zeros_like(acc_ref)
        bias_ref[...] = jnp.zeros_like(bias_ref)

    @pl.when(a == 0)
    def _():
        x_ref[0:chans] = xl_ref[0]
        x_ref[chans : 2 * chans] = xm_ref[0]
        x_ref[2 * chans :] = xr_ref[0]

    @pl.when((d >= 0) & (d < depth))
    def _():
        g = g_ref[0]
        for b in range(3):
            win = x_ref[:, pl.ds(128 * b, lanes)]
            acc_ref[a, b] += lax.dot_general(
                win, g, (((1,), (1,)), ((), ())), preferred_element_type=jnp.float32
            )

    @pl.when(a == 1)
    def _():
        sums = jnp.sum(g_ref[0].astype(jnp.float32), axis=1, keepdims=True)
        bias_ref[...] += jnp.broadcast_to(sums, bias_ref.shape)

    @pl.when((e == depth - 1) & (a == 2))
    def _():
        for ta in range(3):
            for tb in range(3):
                at = (ta * 3 + tb) * rows3
                o_ref[:, at : at + rows3] = acc_ref[ta, tb].T
        o_ref[:, 9 * rows3 :] = bias_ref[...]


def wgrad(xl, xm, xr, gp):
    depth, chans, lanes_h = xm.shape
    lanes = gp.shape[2]
    rows3 = 3 * chans
    width_out = 9 * rows3 + 128
    cost = pl.CostEstimate(
        flops=2 * 9 * depth * rows3 * chans * lanes,
        bytes_accessed=xm.size * 6 + gp.size * 2 * 3 + chans * width_out * 4,
        transcendentals=0,
    )
    return pl.pallas_call(
        functools.partial(_wgrad_kernel, depth, lanes),
        grid=(depth, 3),
        in_specs=[
            pl.BlockSpec((1, chans, lanes_h), lambda e, a: (e, 0, 0)),
            pl.BlockSpec((1, chans, lanes_h), lambda e, a: (e, 0, 0)),
            pl.BlockSpec((1, chans, lanes_h), lambda e, a: (e, 0, 0)),
            pl.BlockSpec(
                (1, chans, lanes),
                lambda e, a: (jnp.clip(e + 1 - a, 0, depth - 1), 0, 0),
            ),
        ],
        out_specs=pl.BlockSpec((chans, width_out), lambda e, a: (0, 0)),
        out_shape=jax.ShapeDtypeStruct((chans, width_out), jnp.float32),
        scratch_shapes=[
            pltpu.VMEM((rows3, lanes_h), jnp.bfloat16),
            pltpu.VMEM((3, 3, rows3, chans), jnp.float32),
            pltpu.VMEM((chans, 128), jnp.float32),
        ],
        compiler_params=pltpu.CompilerParams(
            dimension_semantics=("arbitrary", "arbitrary"),
            vmem_limit_bytes=60 * 1024 * 1024,
        ),
        cost_estimate=cost,
    )(xl, xm, xr, gp)


def local(activations, filters, bias, cotangent):
    count, channels, depth, rows, width = activations.shape
    n_filt = lax.axis_size("filt")
    n_patch = lax.axis_size("patch")
    owned = channels // n_filt
    piece = owned // n_patch
    scale = 1.0 / math.sqrt(count * n_patch * depth * rows * n_filt * width)
    rimmed = padded_2(activations, (("filt", 3),), 1)
    accum = lax.conv_general_dilated(
        rimmed,
        filters,
        window_strides=(1, 1, 1),
        padding=((1, 1), (0, 0), (1, 1)),
        dimension_numbers=("NCDHW", "DHWIO", "NCDHW"),
        preferred_element_type=jnp.float32,
    )
    output = (accum + bias.astype(jnp.float32)[None, :, None, None, None]).astype(jnp.bfloat16)
    lanes_h = (rows + 2) * width
    flat = jnp.transpose(rimmed[0], (1, 0, 2, 3)).reshape(depth, channels, lanes_h)
    wide = jnp.pad(flat, ((0, 0), (0, 0), (1, 1)))
    column = lax.broadcasted_iota(jnp.int32, (1, 1, lanes_h), 2) % width
    zero = jnp.zeros((), flat.dtype)
    left = jnp.where(column == 0, zero, wide[..., 0:lanes_h])
    right = jnp.where(column == width - 1, zero, wide[..., 2 : lanes_h + 2])
    gp = cotangent[0].reshape(n_filt, n_patch, piece, depth, rows, width)
    gp = jnp.transpose(gp, (3, 1, 0, 2, 4, 5)).reshape(depth, channels, rows * width)
    grads_t = wgrad(left, flat, right, gp)
    span = grads_t.shape[1]
    taps = 27 * channels
    grads = grads_t.reshape(n_patch * n_filt, piece, span)
    grads = lax.psum_scatter(grads, ("patch", "filt"), scatter_dimension=0, tiled=True)
    grads = lax.all_gather(grads, "patch", axis=0, tiled=True)
    bias_part = grads[:, :, taps].reshape(owned)
    grads = grads[:, :, :taps].reshape(owned, 27, channels)
    filter_grad = jnp.transpose(grads, (1, 2, 0)).reshape(3, 3, 3, channels, owned) * scale
    return (output, filter_grad, bias_part * scale)


def solution(mesh):
    return jax.shard_map(
        local,
        mesh=mesh,
        in_specs=(
            P(("groups", "patch"), None, None, "filt", None),
            P(),
            P(),
            P(("groups", "patch"), None, None, "filt", None),
        ),
        out_specs=(
            P(("groups", "patch"), None, None, "filt", None),
            P("groups", None, None, None, "filt"),
            P(("groups", "filt")),
        ),
        check_vma=False,
    )
```

```python
import functools
import math

import jax
import jax.numpy as jnp
from jax import lax
from jax.experimental import pallas as pl
from jax.experimental.pallas import tpu as pltpu
from jax.sharding import PartitionSpec as P


def padded_2(cells, sides, width):
    for axis, dim in sides:
        count = lax.axis_size(axis)
        ends = count - 1
        head = lax.slice_in_dim(cells, 0, width, axis=dim)
        tail = lax.slice_in_dim(cells, cells.shape[dim] - width, cells.shape[dim], axis=dim)
        cells = jnp.concatenate(
            [
                lax.ppermute(tail, axis, [(i, (i + 1) % count) for i in range(ends)]),
                cells,
                lax.ppermute(head, axis, [((i + 1) % count, i) for i in range(ends)]),
            ],
            axis=dim,
        )
    return cells


def _wgrad_kernel(depth, lanes, blocks, xl_ref, xm_ref, xr_ref, g_ref, o_ref, x_ref, acc_ref, bias_ref):
    e = pl.program_id(0)
    a = pl.program_id(1)
    d = e + 1 - a
    chans = xm_ref.shape[1]
    rows3 = 3 * chans

    @pl.when((e == 0) & (a == 0))
    def _():
        acc_ref[...] = jnp.zeros_like(acc_ref)
        bias_ref[...] = jnp.zeros_like(bias_ref)

    @pl.when(a == 0)
    def _():
        x_ref[0:chans] = xl_ref[0]
        x_ref[chans : 2 * chans] = xm_ref[0]
        x_ref[2 * chans :] = xr_ref[0]

    @pl.when((d >= 0) & (d < depth))
    def _():
        g = g_ref[0]
        for b in range(3):
            win = x_ref[:, pl.ds(128 * b, lanes)]
            acc_ref[a, b] += lax.dot_general(
                win, g, (((1,), (1,)), ((), ())), preferred_element_type=jnp.float32
            )

    @pl.when(a == 1)
    def _():
        sums = jnp.sum(g_ref[0].astype(jnp.float32), axis=1, keepdims=True)
        bias_ref[...] += jnp.broadcast_to(sums, bias_ref.shape)

    @pl.when((e == depth - 1) & (a == 2))
    def _():
        for ta in range(3):
            for tb in range(3):
                at = (ta * 3 + tb) * rows3
                tr = acc_ref[ta, tb].T
                for src, dst, size in blocks:
                    o_ref[dst : dst + size, at : at + rows3] = tr[src : src + size]
        for src, dst, size in blocks:
            o_ref[dst : dst + size, 9 * rows3 :] = bias_ref[src : src + size]


def wgrad(xl, xm, xr, gp, blocks=None):
    depth, chans, lanes_h = xm.shape
    lanes = gp.shape[2]
    rows3 = 3 * chans
    blocks = tuple(blocks) if blocks else ((0, 0, chans),)
    width_out = 9 * rows3 + 128
    cost = pl.CostEstimate(
        flops=2 * 9 * depth * rows3 * chans * lanes,
        bytes_accessed=xm.size * 6 + gp.size * 2 * 3 + chans * width_out * 4,
        transcendentals=0,
    )
    return pl.pallas_call(
        functools.partial(_wgrad_kernel, depth, lanes, blocks),
        grid=(depth, 3),
        in_specs=[
            pl.BlockSpec((1, chans, lanes_h), lambda e, a: (e, 0, 0)),
            pl.BlockSpec((1, chans, lanes_h), lambda e, a: (e, 0, 0)),
            pl.BlockSpec((1, chans, lanes_h), lambda e, a: (e, 0, 0)),
            pl.BlockSpec(
                (1, chans, lanes),
                lambda e, a: (jnp.clip(e + 1 - a, 0, depth - 1), 0, 0),
            ),
        ],
        out_specs=pl.BlockSpec((chans, width_out), lambda e, a: (0, 0)),
        out_shape=jax.ShapeDtypeStruct((chans, width_out), jnp.float32),
        scratch_shapes=[
            pltpu.VMEM((rows3, lanes_h), jnp.bfloat16),
            pltpu.VMEM((3, 3, rows3, chans), jnp.float32),
            pltpu.VMEM((chans, 128), jnp.float32),
        ],
        compiler_params=pltpu.CompilerParams(
            dimension_semantics=("arbitrary", "arbitrary"),
            vmem_limit_bytes=60 * 1024 * 1024,
        ),
        cost_estimate=cost,
    )(xl, xm, xr, gp)


def local(activations, filters, bias, cotangent):
    count, channels, depth, rows, width = activations.shape
    n_filt = lax.axis_size("filt")
    n_patch = lax.axis_size("patch")
    owned = channels // n_filt
    piece = owned // n_patch
    scale = 1.0 / math.sqrt(count * n_patch * depth * rows * n_filt * width)
    rimmed = padded_2(activations, (("filt", 3),), 1)
    accum = lax.conv_general_dilated(
        rimmed,
        filters,
        window_strides=(1, 1, 1),
        padding=((1, 1), (0, 0), (1, 1)),
        dimension_numbers=("NCDHW", "DHWIO", "NCDHW"),
        preferred_element_type=jnp.float32,
    )
    output = (accum + bias.astype(jnp.float32)[None, :, None, None, None]).astype(jnp.bfloat16)
    lanes_h = (rows + 2) * width
    flat = jnp.transpose(rimmed[0], (1, 0, 2, 3)).reshape(depth, channels, lanes_h)
    wide = jnp.pad(flat, ((0, 0), (0, 0), (1, 1)))
    column = lax.broadcasted_iota(jnp.int32, (1, 1, lanes_h), 2) % width
    zero = jnp.zeros((), flat.dtype)
    left = jnp.where(column == 0, zero, wide[..., 0:lanes_h])
    right = jnp.where(column == width - 1, zero, wide[..., 2 : lanes_h + 2])
    if piece % 8 == 0:
        blocks = [
            ((f * n_patch + p) * piece, (p * n_filt + f) * piece, piece)
            for f in range(n_filt)
            for p in range(n_patch)
        ]
        gp = jnp.transpose(cotangent[0], (1, 0, 2, 3)).reshape(depth, channels, rows * width)
    else:
        blocks = None
        gp = cotangent[0].reshape(n_filt, n_patch, piece, depth, rows, width)
        gp = jnp.transpose(gp, (3, 1, 0, 2, 4, 5)).reshape(depth, channels, rows * width)
    grads_t = wgrad(left, flat, right, gp, blocks)
    span = grads_t.shape[1]
    taps = 27 * channels
    grads = grads_t.reshape(n_patch * n_filt, piece, span)
    grads = lax.psum_scatter(grads, ("patch", "filt"), scatter_dimension=0, tiled=True)
    grads = lax.all_gather(grads, "patch", axis=0, tiled=True)
    bias_part = grads[:, :, taps].reshape(owned)
    grads = grads[:, :, :taps].reshape(owned, 27, channels)
    filter_grad = jnp.transpose(grads, (1, 2, 0)).reshape(3, 3, 3, channels, owned) * scale
    return (output, filter_grad, bias_part * scale)


def solution(mesh):
    return jax.shard_map(
        local,
        mesh=mesh,
        in_specs=(
            P(("groups", "patch"), None, None, "filt", None),
            P(),
            P(),
            P(("groups", "patch"), None, None, "filt", None),
        ),
        out_specs=(
            P(("groups", "patch"), None, None, "filt", None),
            P("groups", None, None, None, "filt"),
            P(("groups", "filt")),
        ),
        check_vma=False,
    )
```
